768 devices in a mesh: tok: 96 (over x, z, core), mdl: 8 (over y).
Axes of the slice: x: 4, y: 8, z: 12, core: 2. Of those that a mesh axis runs over, the one named last changes fastest.
Arguments:
- hidden: bfloat16 [8, 24576, 5120], P('mdl', 'tok'), may hold values from -6 to 6
- sketch: bfloat16 [5120, 256], replicated, may hold values from -0.078125 to 0.078125
Outputs:
- cross_gram: float32 [2048, 2048], P('mdl')
- similarity: float32 [8, 8], P('mdl')
The draws below stay inside these ranges and needn't reach their ends.
All inputs are finite; a program needn't handle non-finite values.
Results may differ from the reference program's by a relative error of at most 0.0025.
Values may be sent and summed in bfloat16 or wider, within the bound.
No kernel may reach another device: no remote copies, remote signals or barrier semaphores. Data moves between devices by JAX's collectives and lax.ppermute only.
A program may use at most 64 MiB of HBM per device.

```python
import jax
import jax.numpy as jnp
from jax import lax

D = 5120
K = 256
TOKENS = 24576
MODELS = 8


def draw_hidden(key, part):
    common_key = jax.random.fold_in(key, 101)
    private_key = jax.random.fold_in(key, 202)
    portion_key = jax.random.fold_in(key, 303)
    common = jax.random.normal(common_key, (TOKENS, D), jnp.float32)
    private = jax.random.normal(private_key, (MODELS, TOKENS, D), jnp.float32)
    portion = jax.random.uniform(portion_key, (MODELS, 1, D), jnp.float32, 0.2, 0.9)
    blended = portion * common[None] + jnp.sqrt(1.0 - portion * portion) * private
    return jnp.clip(blended, -6.0, 6.0).astype(jnp.bfloat16)


def gaussian(key, shape, scale, reach, kind=jnp.bfloat16):
    array = scale * jax.random.normal(key, shape, jnp.float32)
    return jnp.clip(array, min=-reach, max=reach).astype(kind)


def setup_inputs(seed: int = 0) -> dict:
    arg_keys = jax.random.split(jax.random.key(seed), 3)
    hidden = draw_hidden(jax.random.fold_in(arg_keys[2], 71), 0)
    sketch = gaussian(arg_keys[1], (D, K), D ** -0.5, 0.078125)
    return dict(hidden=hidden, sketch=sketch)


def project_states(states, sketch):
    return jnp.dot(states.astype(jnp.float32), sketch.astype(jnp.float32), preferred_element_type=jnp.float32).astype(jnp.bfloat16)

def left_solve(factor, block_row):
    width = block_row.shape[0]
    flat_row = block_row.reshape(width, -1)
    solved = lax.linalg.triangular_solve(factor, flat_row, left_side=True, lower=True)
    return solved.reshape(block_row.shape)

def right_solve(factor, block):
    return lax.linalg.triangular_solve(factor, block, left_side=False, lower=True, transpose_a=True)

def reference(hidden, sketch):
    projected = lax.map(lambda states: project_states(states, sketch), hidden)
    models = projected.shape[0]
    basis_width = projected.shape[2]
    stacked = jnp.transpose(projected, (1, 0, 2)).reshape(projected.shape[1], models * basis_width)
    cross_sums = jnp.dot(stacked.T.astype(jnp.float32), stacked.astype(jnp.float32), preferred_element_type=jnp.float32)
    cross_sums = cross_sums.reshape(models, basis_width, models, basis_width)
    grams = jnp.stack([cross_sums[index, :, index, :] for index in range(models)])
    factors = jax.vmap(jnp.linalg.cholesky)(grams)
    left_done = jax.vmap(left_solve)(factors, cross_sums)

    def right_row(block_row):
        return jax.vmap(right_solve, in_axes=(0, 1), out_axes=1)(factors, block_row)
    right_done = jax.vmap(right_row)(left_done)
    cross_gram = right_done.reshape(models * basis_width, models * basis_width)
    similarity = jnp.sum(right_done * right_done, axis=(1, 3)) / basis_width
    return (cross_gram, similarity)
```

```python
import jax
import jax.numpy as jnp
from jax import lax
from jax.sharding import Mesh
from jax.sharding import PartitionSpec as P

HIGH = lax.Precision.HIGHEST


def scatter_sum(chunks, axes):
    return lax.all_to_all(chunks, axes, 0, 0, tiled=True).sum(axis=0)


def gather_all(piece, axes, count):
    copies = jnp.broadcast_to(piece[None], (count,) + piece.shape)
    return lax.all_to_all(copies, axes, 0, 0, tiled=True)


def sum_over_tokens(row, inner, outer):
    rows, cols = row.shape
    n_in = lax.axis_size(inner)
    n_out = lax.axis_size(outer)
    width = cols // n_in
    part = scatter_sum(row.reshape(rows, n_in, width).transpose(1, 0, 2), inner)
    pad = (-rows) % n_out
    padded = jnp.pad(part, ((0, pad), (0, 0))).reshape(n_out, (rows + pad) // n_out, width)
    piece = scatter_sum(padded, outer)
    part = gather_all(piece, outer, n_out).reshape(rows + pad, width)[:rows]
    full = gather_all(part, inner, n_in)
    return full.transpose(1, 0, 2).reshape(rows, cols)


def on_device(hidden, sketch):
    states = hidden[0]
    projected = jnp.dot(states, sketch, preferred_element_type=jnp.float32).astype(jnp.bfloat16)
    basis_width = projected.shape[1]
    models = lax.axis_size("mdl")
    me = lax.axis_index("mdl")
    everyone = gather_all(projected, "mdl", models)
    everyone = everyone.transpose(1, 0, 2).reshape(projected.shape[0], models * basis_width)
    local_row = jnp.dot(projected.T, everyone, preferred_element_type=jnp.float32)
    row_sums = sum_over_tokens(local_row, ("x", "c"), "z")
    row_tiles = row_sums.reshape(basis_width, models, basis_width)
    gram_total = lax.dynamic_index_in_dim(row_tiles, me, 1, keepdims=False)
    factor = jnp.linalg.cholesky(gram_total)
    eye = jnp.eye(basis_width, dtype=jnp.float32)
    inverse = lax.linalg.triangular_solve(factor, eye, left_side=True, lower=True)
    inverses = gather_all(inverse, "mdl", models)
    left_done = jnp.einsum("ab,bjc->ajc", inverse, row_tiles, precision=HIGH)
    right_done = jnp.einsum("ajc,jdc->ajd", left_done, inverses, precision=HIGH)
    cross_gram = right_done.reshape(basis_width, models * basis_width)
    similarity = jnp.sum(right_done * right_done, axis=(0, 2)) / basis_width
    return (cross_gram, similarity[None, :])


def solution(mesh):
    tok_size = mesh.shape["tok"]
    cores = 2
    z_size = tok_size // (4 * cores)
    devices = mesh.devices.reshape(tok_size // (z_size * cores), z_size, cores, mesh.shape["mdl"])
    sub = Mesh(devices, ("x", "z", "c", "mdl"))
    return jax.shard_map(
        on_device,
        mesh=sub,
        in_specs=(P("mdl", ("x", "z", "c"), None), P()),
        out_specs=(P("mdl", None), P("mdl", None)),
        check_vma=False,
    )
```

```python
import jax
import jax.numpy as jnp
from jax import lax
from jax.sharding import Mesh
from jax.sharding import PartitionSpec as P

HIGH = lax.Precision.HIGHEST


def scatter_sum(chunks, axes):
    return lax.all_to_all(chunks, axes, 0, 0, tiled=True).sum(axis=0)


def gather_all(piece, axes, count):
    copies = jnp.broadcast_to(piece[None], (count,) + piece.shape)
    return lax.all_to_all(copies, axes, 0, 0, tiled=True)


def sum_over_tokens(row, inner, outer):
    rows, cols = row.shape
    n_in = lax.axis_size(inner)
    n_out = lax.axis_size(outer)
    width = cols // n_in
    part = scatter_sum(row.reshape(rows, n_in, width).transpose(1, 0, 2), inner)
    pad = (-rows) % n_out
    padded = jnp.pad(part, ((0, pad), (0, 0))).reshape(n_out, (rows + pad) // n_out, width)
    piece = scatter_sum(padded, outer)
    part = gather_all(piece, outer, n_out).reshape(rows + pad, width)[:rows]
    full = gather_all(part, inner, n_in)
    return full.transpose(1, 0, 2).reshape(rows, cols)


def pack_lower(m):
    h = m.shape[0] // 2
    top, low_right = m[:h, :h], m[h:, h:]
    folded = jnp.tril(top, -1) + low_right.T
    return jnp.concatenate([m[h:, :h], folded, jnp.diagonal(top)[None]], axis=0)


def unpack_lower(p):
    h = p.shape[-1]
    low_left, folded, diag = p[..., :h, :], p[..., h:2 * h, :], p[..., 2 * h, :]
    top = jnp.tril(folded, -1) + diag[..., :, None] * jnp.eye(h, dtype=p.dtype)
    low_right = jnp.swapaxes(jnp.triu(folded), -1, -2)
    upper = jnp.concatenate([top, jnp.zeros_like(top)], axis=-1)
    lower = jnp.concatenate([low_left, low_right], axis=-1)
    return jnp.concatenate([upper, lower], axis=-2)


def on_device(hidden, sketch):
    states = hidden[0]
    projected = jnp.dot(states, sketch, preferred_element_type=jnp.float32).astype(jnp.bfloat16)
    basis_width = projected.shape[1]
    models = lax.axis_size("mdl")
    me = lax.axis_index("mdl")
    everyone = gather_all(projected, "mdl", models)
    everyone = everyone.transpose(1, 0, 2).reshape(projected.shape[0], models * basis_width)
    local_row = jnp.dot(projected.T, everyone, preferred_element_type=jnp.float32)
    row_sums = sum_over_tokens(local_row, ("x", "c"), "z")
    row_tiles = row_sums.reshape(basis_width, models, basis_width)
    gram_total = lax.dynamic_index_in_dim(row_tiles, me, 1, keepdims=False)
    factor = jnp.linalg.cholesky(gram_total)
    eye = jnp.eye(basis_width, dtype=jnp.float32)
    inverse = lax.linalg.triangular_solve(factor, eye, left_side=True, lower=True)
    inverses = unpack_lower(gather_all(pack_lower(inverse), "mdl", models))
    left_done = jnp.einsum("ab,bjc->ajc", inverse, row_tiles, precision=HIGH)
    right_done = jnp.einsum("ajc,jdc->ajd", left_done, inverses, precision=HIGH)
    cross_gram = right_done.reshape(basis_width, models * basis_width)
    similarity = jnp.sum(right_done * right_done, axis=(0, 2)) / basis_width
    return (cross_gram, similarity[None, :])


def solution(mesh):
    tok_size = mesh.shape["tok"]
    cores = 2
    z_size = tok_size // (4 * cores)
    devices = mesh.devices.reshape(tok_size // (z_size * cores), z_size, cores, mesh.shape["mdl"])
    sub = Mesh(devices, ("x", "z", "c", "mdl"))
    return jax.shard_map(
        on_device,
        mesh=sub,
        in_specs=(P("mdl", ("x", "z", "c"), None), P()),
        out_specs=(P("mdl", None), P("mdl", None)),
        check_vma=False,
    )
```

```python
import jax
import jax.numpy as jnp
from jax import lax
from jax.sharding import Mesh
from jax.sharding import PartitionSpec as P

HIGH = lax.Precision.HIGHEST


def scatter_sum(chunks, axes):
    return lax.all_to_all(chunks, axes, 0, 0, tiled=True).sum(axis=0)


def gather_all(piece, axes, count):
    copies = jnp.broadcast_to(piece[None], (count,) + piece.shape)
    return lax.all_to_all(copies, axes, 0, 0, tiled=True)


def sum_over_tokens(row, inner, outer):
    rows, cols = row.shape
    n_in = lax.axis_size(inner)
    n_out = lax.axis_size(outer)
    width = cols // n_in
    part = scatter_sum(row.reshape(rows, n_in, width).transpose(1, 0, 2), inner)
    pad = (-rows) % n_out
    padded = jnp.pad(part, ((0, pad), (0, 0))).reshape(n_out, (rows + pad) // n_out, width)
    piece = scatter_sum(padded, outer)
    part = gather_all(piece, outer, n_out).reshape(rows + pad, width)[:rows]
    full = gather_all(part, inner, n_in)
    return full.transpose(1, 0, 2).reshape(rows, cols)


def pack_lower(m):
    h = m.shape[0] // 2
    top, low_right = m[:h, :h], m[h:, h:]
    folded = jnp.tril(top, -1) + low_right.T
    return jnp.concatenate([m[h:, :h], folded, jnp.diagonal(top)[None]], axis=0)


def unpack_lower(p):
    h = p.shape[-1]
    low_left, folded, diag = p[..., :h, :], p[..., h:2 * h, :], p[..., 2 * h, :]
    top = jnp.tril(folded, -1) + diag[..., :, None] * jnp.eye(h, dtype=p.dtype)
    low_right = jnp.swapaxes(jnp.triu(folded), -1, -2)
    upper = jnp.concatenate([top, jnp.zeros_like(top)], axis=-1)
    lower = jnp.concatenate([low_left, low_right], axis=-1)
    return jnp.concatenate([upper, lower], axis=-2)


def to_halves(a):
    w = a.shape[-1] // 2
    return jnp.concatenate([a[..., :w], a[..., w:]], axis=-2)


def symmetric(lower):
    return lower + lower.T - jnp.diag(jnp.diagonal(lower))


def on_device(hidden, sketch):
    states = hidden[0]
    projected = jnp.dot(states, sketch, preferred_element_type=jnp.float32).astype(jnp.bfloat16)
    tokens, width = projected.shape
    models = lax.axis_size("mdl")
    me = lax.axis_index("mdl")
    inner, outer = ("x", "c"), "z"
    n_out = lax.axis_size(outer)
    assert lax.axis_size(inner) == models
    everyone = gather_all(projected, "mdl", models)
    local_row = jnp.einsum("ta,jtc->jac", projected, everyone, preferred_element_type=jnp.float32)
    local_grams = jnp.einsum("jta,jtc->jac", everyone, everyone, preferred_element_type=jnp.float32)
    packed_grams = jax.vmap(pack_lower)(jnp.tril(local_grams))
    payload = jnp.concatenate([to_halves(local_row), packed_grams], axis=1)
    part = scatter_sum(payload, inner)
    rows = part.shape[0]
    pad = (-rows) % n_out
    padded = jnp.pad(part, ((0, pad), (0, 0))).reshape(n_out, (rows + pad) // n_out, part.shape[1])
    piece = scatter_sum(padded, outer)
    part = gather_all(piece, outer, n_out).reshape(rows + pad, part.shape[1])[:rows]
    half = width // 2
    tile = jnp.concatenate([part[:width], part[width:2 * width]], axis=1)
    gram = symmetric(unpack_lower(part[2 * width:]))
    factor = jnp.linalg.cholesky(gram)
    eye = jnp.eye(width, dtype=jnp.float32)
    inverse = lax.linalg.triangular_solve(factor, eye, left_side=True, lower=True)
    right_done = jnp.dot(tile, inverse.T, precision=HIGH)
    sent = jnp.concatenate([to_halves(right_done), pack_lower(inverse)], axis=0)
    got = gather_all(sent, inner, models)
    row = got[:, :2 * width].reshape(models, 2, width, half).transpose(2, 0, 1, 3).reshape(width, models, width)
    inverses = unpack_lower(got[:, 2 * width:])
    mine = lax.dynamic_index_in_dim(inverses, me, 0, keepdims=False)
    done = jnp.einsum("ab,bkc->akc", mine, row, precision=HIGH)
    cross_gram = done.reshape(width, models * width)
    similarity = jnp.sum(done * done, axis=(0, 2)) / width
    return (cross_gram, similarity[None, :])


def solution(mesh):
    tok_size = mesh.shape["tok"]
    cores = 2
    z_size = tok_size // (4 * cores)
    devices = mesh.devices.reshape(tok_size // (z_size * cores), z_size, cores, mesh.shape["mdl"])
    sub = Mesh(devices, ("x", "z", "c", "mdl"))
    return jax.shard_map(
        on_device,
        mesh=sub,
        in_specs=(P("mdl", ("x", "z", "c"), None), P()),
        out_specs=(P("mdl", None), P("mdl", None)),
        check_vma=False,
    )
```

```python
import jax
import jax.numpy as jnp
from jax import lax
from jax.sharding import Mesh
from jax.sharding import PartitionSpec as P

HIGH = lax.Precision.HIGHEST


def scatter_sum(chunks, axes):
    return lax.all_to_all(chunks, axes, 0, 0, tiled=True).sum(axis=0)


def gather_all(piece, axes, count):
    copies = jnp.broadcast_to(piece[None], (count,) + piece.shape)
    return lax.all_to_all(copies, axes, 0, 0, tiled=True)


def swap_halves_sum(row, axis):
    cols = row.shape[1]
    side = lax.axis_index(axis)
    halves = row.reshape(row.shape[0], 2, cols // 2)
    mine = lax.dynamic_index_in_dim(halves, side, 1, keepdims=False)
    theirs = lax.dynamic_index_in_dim(halves, 1 - side, 1, keepdims=False)
    return mine + lax.ppermute(theirs, axis, [(0, 1), (1, 0)])


def swap_halves_join(half, axis):
    side = lax.axis_index(axis)
    other = lax.ppermute(half, axis, [(0, 1), (1, 0)])
    return jnp.where(side == 0, jnp.concatenate([half, other], 1), jnp.concatenate([other, half], 1))


def sum_over_tokens(row, pair, ring, outer):
    rows = row.shape[0]
    n_ring = lax.axis_size(ring)
    n_out = lax.axis_size(outer)
    part = swap_halves_sum(row, pair)
    width = part.shape[1] // n_ring
    part = scatter_sum(part.reshape(rows, n_ring, width).transpose(1, 0, 2), ring)
    pad = (-rows) % n_out
    padded = jnp.pad(part, ((0, pad), (0, 0))).reshape(n_out, (rows + pad) // n_out, width)
    piece = scatter_sum(padded, outer)
    part = gather_all(piece, outer, n_out).reshape(rows + pad, width)[:rows]
    part = gather_all(part, ring, n_ring).transpose(1, 0, 2).reshape(rows, n_ring * width)
    return swap_halves_join(part, pair)


def pack_lower(m):
    h = m.shape[0] // 2
    top, low_right = m[:h, :h], m[h:, h:]
    folded = jnp.tril(top, -1) + low_right.T
    return jnp.concatenate([m[h:, :h], folded, jnp.diagonal(top)[None]], axis=0)


def unpack_lower(p):
    h = p.shape[-1]
    low_left, folded, diag = p[..., :h, :], p[..., h:2 * h, :], p[..., 2 * h, :]
    top = jnp.tril(folded, -1) + diag[..., :, None] * jnp.eye(h, dtype=p.dtype)
    low_right = jnp.swapaxes(jnp.triu(folded), -1, -2)
    upper = jnp.concatenate([top, jnp.zeros_like(top)], axis=-1)
    lower = jnp.concatenate([low_left, low_right], axis=-1)
    return jnp.concatenate([upper, lower], axis=-2)


def on_device(hidden, sketch):
    states = hidden[0]
    projected = jnp.dot(states, sketch, preferred_element_type=jnp.float32).astype(jnp.bfloat16)
    basis_width = projected.shape[1]
    models = lax.axis_size("mdl")
    me = lax.axis_index("mdl")
    everyone = gather_all(projected, "mdl", models)
    everyone = everyone.transpose(1, 0, 2).reshape(projected.shape[0], models * basis_width)
    local_row = jnp.dot(projected.T, everyone, preferred_element_type=jnp.float32)
    row_sums = sum_over_tokens(local_row, "c", "x", "z")
    row_tiles = row_sums.reshape(basis_width, models, basis_width)
    gram_total = lax.dynamic_index_in_dim(row_tiles, me, 1, keepdims=False)
    factor = jnp.linalg.cholesky(gram_total)
    eye = jnp.eye(basis_width, dtype=jnp.float32)
    inverse = lax.linalg.triangular_solve(factor, eye, left_side=True, lower=True)
    inverses = unpack_lower(gather_all(pack_lower(inverse), "mdl", models))
    left_done = jnp.einsum("ab,bjc->ajc", inverse, row_tiles, precision=HIGH)
    right_done = jnp.einsum("ajc,jdc->ajd", left_done, inverses, precision=HIGH)
    cross_gram = right_done.reshape(basis_width, models * basis_width)
    similarity = jnp.sum(right_done * right_done, axis=(0, 2)) / basis_width
    return (cross_gram, similarity[None, :])


def solution(mesh):
    tok_size = mesh.shape["tok"]
    cores = 2
    z_size = tok_size // (4 * cores)
    devices = mesh.devices.reshape(tok_size // (z_size * cores), z_size, cores, mesh.shape["mdl"])
    sub = Mesh(devices, ("x", "z", "c", "mdl"))
    return jax.shard_map(
        on_device,
        mesh=sub,
        in_specs=(P("mdl", ("x", "z", "c"), None), P()),
        out_specs=(P("mdl", None), P("mdl", None)),
        check_vma=False,
    )
```

```python
import jax
import jax.numpy as jnp
from jax import lax
from jax.sharding import Mesh
from jax.sharding import PartitionSpec as P

HIGH = lax.Precision.HIGHEST


def scatter_sum(chunks, axes):
    return lax.all_to_all(chunks, axes, 0, 0, tiled=True).sum(axis=0)


def gather_all(piece, axes, count):
    copies = jnp.broadcast_to(piece[None], (count,) + piece.shape)
    return lax.all_to_all(copies, axes, 0, 0, tiled=True)


def swap_halves_sum(row, axis):
    cols = row.shape[1]
    side = lax.axis_index(axis)
    halves = row.reshape(row.shape[0], 2, cols // 2)
    mine = lax.dynamic_index_in_dim(halves, side, 1, keepdims=False)
    theirs = lax.dynamic_index_in_dim(halves, 1 - side, 1, keepdims=False)
    return mine + lax.ppermute(theirs, axis, [(0, 1), (1, 0)])


def swap_halves_join(half, axis):
    side = lax.axis_index(axis)
    other = lax.ppermute(half, axis, [(0, 1), (1, 0)])
    return jnp.where(side == 0, jnp.concatenate([half, other], 1), jnp.concatenate([other, half], 1))


def sum_over_tokens(row, pair, ring, outer):
    rows = row.shape[0]
    n_ring = lax.axis_size(ring)
    n_out = lax.axis_size(outer)
    part = swap_halves_sum(row, pair)
    width = part.shape[1] // n_ring
    part = scatter_sum(part.reshape(rows, n_ring, width).transpose(1, 0, 2), ring)
    pad = (-rows) % n_out
    padded = jnp.pad(part, ((0, pad), (0, 0))).reshape(n_out, (rows + pad) // n_out, width)
    piece = scatter_sum(padded, outer)
    part = gather_all(piece, outer, n_out).reshape(rows + pad, width)[:rows]
    part = gather_all(part, ring, n_ring).transpose(1, 0, 2).reshape(rows, n_ring * width)
    return swap_halves_join(part, pair)


def pack_lower(m):
    h = m.shape[0] // 2
    top, low_right = m[:h, :h], m[h:, h:]
    folded = jnp.tril(top, -1) + low_right.T
    return jnp.concatenate([m[h:, :h], folded, jnp.diagonal(top)[None]], axis=0)


def unpack_lower(p):
    h = p.shape[-1]
    low_left, folded, diag = p[..., :h, :], p[..., h:2 * h, :], p[..., 2 * h, :]
    top = jnp.tril(folded, -1) + diag[..., :, None] * jnp.eye(h, dtype=p.dtype)
    low_right = jnp.swapaxes(jnp.triu(folded), -1, -2)
    upper = jnp.concatenate([top, jnp.zeros_like(top)], axis=-1)
    lower = jnp.concatenate([low_left, low_right], axis=-1)
    return jnp.concatenate([upper, lower], axis=-2)


def factor_inverse(gram):
    h = gram.shape[0] // 2
    eye = jnp.eye(h, dtype=gram.dtype)
    top = jnp.linalg.cholesky(gram[:h, :h])
    top_inv = lax.linalg.triangular_solve(top, eye, left_side=True, lower=True)
    low_left = jnp.dot(gram[h:, :h], top_inv.T, precision=HIGH)
    rest = gram[h:, h:] - jnp.dot(low_left, low_left.T, precision=HIGH)
    low = jnp.linalg.cholesky(rest)
    low_inv = lax.linalg.triangular_solve(low, eye, left_side=True, lower=True)
    mixed = -jnp.dot(low_inv, jnp.dot(low_left, top_inv, precision=HIGH), precision=HIGH)
    upper = jnp.concatenate([top_inv, jnp.zeros_like(top_inv)], axis=1)
    lower = jnp.concatenate([mixed, low_inv], axis=1)
    return jnp.concatenate([upper, lower], axis=0)


def on_device(hidden, sketch):
    states = hidden[0]
    projected = jnp.dot(states, sketch, preferred_element_type=jnp.float32).astype(jnp.bfloat16)
    basis_width = projected.shape[1]
    models = lax.axis_size("mdl")
    me = lax.axis_index("mdl")
    everyone = gather_all(projected, "mdl", models)
    everyone = everyone.transpose(1, 0, 2).reshape(projected.shape[0], models * basis_width)
    local_row = jnp.dot(projected.T, everyone, preferred_element_type=jnp.float32)
    row_sums = sum_over_tokens(local_row, "c", "x", "z")
    row_tiles = row_sums.reshape(basis_width, models, basis_width)
    gram_total = lax.dynamic_index_in_dim(row_tiles, me, 1, keepdims=False)
    inverse = factor_inverse(gram_total)
    inverses = unpack_lower(gather_all(pack_lower(inverse), "mdl", models))
    left_done = jnp.einsum("ab,bjc->ajc", inverse, row_tiles, precision=HIGH)
    right_done = jnp.einsum("ajc,jdc->ajd", left_done, inverses, precision=HIGH)
    cross_gram = right_done.reshape(basis_width, models * basis_width)
    similarity = jnp.sum(right_done * right_done, axis=(0, 2)) / basis_width
    return (cross_gram, similarity[None, :])


def solution(mesh):
    tok_size = mesh.shape["tok"]
    cores = 2
    z_size = tok_size // (4 * cores)
    devices = mesh.devices.reshape(tok_size // (z_size * cores), z_size, cores, mesh.shape["mdl"])
    sub = Mesh(devices, ("x", "z", "c", "mdl"))
    return jax.shard_map(
        on_device,
        mesh=sub,
        in_specs=(P("mdl", ("x", "z", "c"), None), P()),
        out_specs=(P("mdl", None), P("mdl", None)),
        check_vma=False,
    )
```

```python
import jax
import jax.numpy as jnp
from jax import lax
from jax.sharding import Mesh
from jax.sharding import PartitionSpec as P

HIGH = lax.Precision.HIGHEST


def scatter_sum(chunks, axes):
    return lax.all_to_all(chunks, axes, 0, 0, tiled=True).sum(axis=0)


def gather_all(piece, axes, count):
    copies = jnp.broadcast_to(piece[None], (count,) + piece.shape)
    return lax.all_to_all(copies, axes, 0, 0, tiled=True)


def swap_halves_sum(row, axis):
    side = lax.axis_index(axis)
    halves = row.reshape(2, row.shape[0] // 2, row.shape[1])
    mine = lax.dynamic_index_in_dim(halves, side, 0, keepdims=False)
    theirs = lax.dynamic_index_in_dim(halves, 1 - side, 0, keepdims=False)
    return mine + lax.ppermute(theirs, axis, [(0, 1), (1, 0)])


def swap_halves_join(half, axis):
    side = lax.axis_index(axis)
    other = lax.ppermute(half, axis, [(0, 1), (1, 0)])
    return jnp.where(side == 0, jnp.concatenate([half, other], 0), jnp.concatenate([other, half], 0))


def sum_over_tokens(row, pair, ring, outer, lanes=128):
    cols = row.shape[1]
    n_ring = lax.axis_size(ring)
    n_out = lax.axis_size(outer)
    part = swap_halves_sum(row, pair)
    rows = part.shape[0] // n_ring
    part = scatter_sum(part.reshape(n_ring, rows, cols), ring)
    flat = part.reshape(rows * cols // lanes, lanes)
    pad = (-flat.shape[0]) % n_out
    padded = jnp.pad(flat, ((0, pad), (0, 0))).reshape(n_out, -1, lanes)
    piece = scatter_sum(padded, outer)
    flat = gather_all(piece, outer, n_out).reshape(-1, lanes)[: flat.shape[0]]
    part = gather_all(flat.reshape(rows, cols), ring, n_ring).reshape(n_ring * rows, cols)
    return swap_halves_join(part, pair)


def pack_lower(m):
    h = m.shape[0] // 2
    top, low_right = m[:h, :h], m[h:, h:]
    folded = jnp.tril(top, -1) + low_right.T
    return jnp.concatenate([m[h:, :h], folded, jnp.diagonal(top)[None]], axis=0)


def unpack_lower(p):
    h = p.shape[-1]
    low_left, folded, diag = p[..., :h, :], p[..., h:2 * h, :], p[..., 2 * h, :]
    top = jnp.tril(folded, -1) + diag[..., :, None] * jnp.eye(h, dtype=p.dtype)
    low_right = jnp.swapaxes(jnp.triu(folded), -1, -2)
    upper = jnp.concatenate([top, jnp.zeros_like(top)], axis=-1)
    lower = jnp.concatenate([low_left, low_right], axis=-1)
    return jnp.concatenate([upper, lower], axis=-2)


def factor_inverse(gram):
    h = gram.shape[0] // 2
    eye = jnp.eye(h, dtype=gram.dtype)
    top = jnp.linalg.cholesky(gram[:h, :h])
    top_inv = lax.linalg.triangular_solve(top, eye, left_side=True, lower=True)
    low_left = jnp.dot(gram[h:, :h], top_inv.T, precision=HIGH)
    rest = gram[h:, h:] - jnp.dot(low_left, low_left.T, precision=HIGH)
    low = jnp.linalg.cholesky(rest)
    low_inv = lax.linalg.triangular_solve(low, eye, left_side=True, lower=True)
    mixed = -jnp.dot(low_inv, jnp.dot(low_left, top_inv, precision=HIGH), precision=HIGH)
    upper = jnp.concatenate([top_inv, jnp.zeros_like(top_inv)], axis=1)
    lower = jnp.concatenate([mixed, low_inv], axis=1)
    return jnp.concatenate([upper, lower], axis=0)


def on_device(hidden, sketch):
    states = hidden[0]
    projected = jnp.dot(states, sketch, preferred_element_type=jnp.float32).astype(jnp.bfloat16)
    basis_width = projected.shape[1]
    models = lax.axis_size("mdl")
    me = lax.axis_index("mdl")
    everyone = gather_all(projected, "mdl", models)
    everyone = everyone.transpose(1, 0, 2).reshape(projected.shape[0], models * basis_width)
    local_row = jnp.dot(projected.T, everyone, preferred_element_type=jnp.float32)
    row_sums = sum_over_tokens(local_row, "c", "x", "z")
    row_tiles = row_sums.reshape(basis_width, models, basis_width)
    gram_total = lax.dynamic_index_in_dim(row_tiles, me, 1, keepdims=False)
    inverse = factor_inverse(gram_total)
    inverses = unpack_lower(gather_all(pack_lower(inverse), "mdl", models))
    left_done = jnp.einsum("ab,bjc->ajc", inverse, row_tiles, precision=lax.Precision.HIGH)
    right_done = jnp.einsum("ajc,jdc->ajd", left_done, inverses, precision=lax.Precision.HIGH)
    cross_gram = right_done.reshape(basis_width, models * basis_width)
    similarity = jnp.sum(right_done * right_done, axis=(0, 2)) / basis_width
    return (cross_gram, similarity[None, :])


def solution(mesh):
    tok_size = mesh.shape["tok"]
    cores = 2
    z_size = tok_size // (4 * cores)
    devices = mesh.devices.reshape(tok_size // (z_size * cores), z_size, cores, mesh.shape["mdl"])
    sub = Mesh(devices, ("x", "z", "c", "mdl"))
    return jax.shard_map(
        on_device,
        mesh=sub,
        in_specs=(P("mdl", ("x", "z", "c"), None), P()),
        out_specs=(P("mdl", None), P("mdl", None)),
        check_vma=False,
    )
```

```python
import jax
import jax.numpy as jnp
from jax import lax
from jax.sharding import Mesh
from jax.sharding import PartitionSpec as P

HIGH = lax.Precision.HIGHEST


def scatter_sum(chunks, axes):
    return lax.all_to_all(chunks, axes, 0, 0, tiled=True).sum(axis=0)


def gather_all(piece, axes, count):
    copies = jnp.broadcast_to(piece[None], (count,) + piece.shape)
    return lax.all_to_all(copies, axes, 0, 0, tiled=True)


def swap_halves_sum(tiles, axis):
    side = lax.axis_index(axis)
    halves = tiles.reshape((2, tiles.shape[0] // 2) + tiles.shape[1:])
    mine = lax.dynamic_index_in_dim(halves, side, 0, keepdims=False)
    theirs = lax.dynamic_index_in_dim(halves, 1 - side, 0, keepdims=False)
    return mine + lax.ppermute(theirs, axis, [(0, 1), (1, 0)])


def swap_halves_join(half, axis):
    side = lax.axis_index(axis)
    other = lax.ppermute(half, axis, [(0, 1), (1, 0)])
    return jnp.where(side == 0, jnp.concatenate([half, other], 0), jnp.concatenate([other, half], 0))


def sum_over_tokens(tiles, pair, ring, outer, lanes=128):
    n_ring = lax.axis_size(ring)
    n_out = lax.axis_size(outer)
    part = swap_halves_sum(tiles, pair)
    each = part.shape[0] // n_ring
    part = scatter_sum(part.reshape((n_ring, each) + part.shape[1:]), ring)
    flat = part.reshape(-1, lanes)
    pad = (-flat.shape[0]) % n_out
    padded = jnp.pad(flat, ((0, pad), (0, 0))).reshape(n_out, -1, lanes)
    piece = scatter_sum(padded, outer)
    flat = gather_all(piece, outer, n_out).reshape(-1, lanes)[: flat.shape[0]]
    part = gather_all(flat.reshape(part.shape), ring, n_ring).reshape((n_ring * each,) + part.shape[1:])
    return swap_halves_join(part, pair)


def pack_lower(m):
    h = m.shape[0] // 2
    top, low_right = m[:h, :h], m[h:, h:]
    folded = jnp.tril(top, -1) + low_right.T
    return jnp.concatenate([m[h:, :h], folded, jnp.diagonal(top)[None]], axis=0)


def unpack_lower(p):
    h = p.shape[-1]
    low_left, folded, diag = p[..., :h, :], p[..., h:2 * h, :], p[..., 2 * h, :]
    top = jnp.tril(folded, -1) + diag[..., :, None] * jnp.eye(h, dtype=p.dtype)
    low_right = jnp.swapaxes(jnp.triu(folded), -1, -2)
    upper = jnp.concatenate([top, jnp.zeros_like(top)], axis=-1)
    lower = jnp.concatenate([low_left, low_right], axis=-1)
    return jnp.concatenate([upper, lower], axis=-2)


def factor_inverse(gram):
    h = gram.shape[0] // 2
    eye = jnp.eye(h, dtype=gram.dtype)
    top = jnp.linalg.cholesky(gram[:h, :h])
    top_inv = lax.linalg.triangular_solve(top, eye, left_side=True, lower=True)
    low_left = jnp.dot(gram[h:, :h], top_inv.T, precision=HIGH)
    rest = gram[h:, h:] - jnp.dot(low_left, low_left.T, precision=HIGH)
    low = jnp.linalg.cholesky(rest)
    low_inv = lax.linalg.triangular_solve(low, eye, left_side=True, lower=True)
    mixed = -jnp.dot(low_inv, jnp.dot(low_left, top_inv, precision=HIGH), precision=HIGH)
    upper = jnp.concatenate([top_inv, jnp.zeros_like(top_inv)], axis=1)
    lower = jnp.concatenate([mixed, low_inv], axis=1)
    return jnp.concatenate([upper, lower], axis=0)


def on_device(hidden, sketch):
    states = hidden[0]
    projected = jnp.dot(states, sketch, preferred_element_type=jnp.float32).astype(jnp.bfloat16)
    basis_width = projected.shape[1]
    models = lax.axis_size("mdl")
    me = lax.axis_index("mdl")
    everyone = gather_all(projected, "mdl", models)
    local_tiles = jnp.einsum("ta,jtc->jac", projected, everyone, preferred_element_type=jnp.float32)
    tiles = sum_over_tokens(local_tiles, "c", "x", "z")
    gram_total = lax.dynamic_index_in_dim(tiles, me, 0, keepdims=False)
    inverse = factor_inverse(gram_total)
    inverses = unpack_lower(gather_all(pack_lower(inverse), "mdl", models))
    left_done = jnp.einsum("ab,jbc->jac", inverse, tiles, precision=lax.Precision.HIGH)
    right_done = jnp.einsum("jac,jdc->jad", left_done, inverses, precision=lax.Precision.HIGH)
    cross_gram = right_done.transpose(1, 0, 2).reshape(basis_width, models * basis_width)
    similarity = jnp.sum(right_done * right_done, axis=(1, 2)) / basis_width
    return (cross_gram, similarity[None, :])


def solution(mesh):
    tok_size = mesh.shape["tok"]
    cores = 2
    z_size = tok_size // (4 * cores)
    devices = mesh.devices.reshape(tok_size // (z_size * cores), z_size, cores, mesh.shape["mdl"])
    sub = Mesh(devices, ("x", "z", "c", "mdl"))
    return jax.shard_map(
        on_device,
        mesh=sub,
        in_specs=(P("mdl", ("x", "z", "c"), None), P()),
        out_specs=(P("mdl", None), P("mdl", None)),
        check_vma=False,
    )
```

```python
import jax
import jax.numpy as jnp
from jax import lax
from jax.sharding import Mesh
from jax.sharding import PartitionSpec as P

HIGH = lax.Precision.HIGHEST


def scatter_sum(chunks, axes):
    return lax.all_to_all(chunks, axes, 0, 0, tiled=True).sum(axis=0)


def gather_all(piece, axes, count):
    copies = jnp.broadcast_to(piece[None], (count,) + piece.shape)
    return lax.all_to_all(copies, axes, 0, 0, tiled=True)


def swap_halves_sum(tiles, axis):
    side = lax.axis_index(axis)
    halves = tiles.reshape((2, tiles.shape[0] // 2) + tiles.shape[1:])
    mine = lax.dynamic_index_in_dim(halves, side, 0, keepdims=False)
    theirs = lax.dynamic_index_in_dim(halves, 1 - side, 0, keepdims=False)
    return mine + lax.ppermute(theirs, axis, [(0, 1), (1, 0)])


def swap_halves_join(half, axis):
    side = lax.axis_index(axis)
    other = lax.ppermute(half, axis, [(0, 1), (1, 0)])
    return jnp.where(side == 0, jnp.concatenate([half, other], 0), jnp.concatenate([other, half], 0))


def sum_over_tokens(tiles, pair, ring, outer, lanes=128):
    n_ring = lax.axis_size(ring)
    n_out = lax.axis_size(outer)
    part = swap_halves_sum(tiles, pair)
    each = part.shape[0] // n_ring
    part = scatter_sum(part.reshape((n_ring, each) + part.shape[1:]), ring)
    flat = part.reshape(-1, lanes)
    pad = (-flat.shape[0]) % n_out
    padded = jnp.pad(flat, ((0, pad), (0, 0))).reshape(n_out, -1, lanes)
    piece = scatter_sum(padded, outer)
    flat = gather_all(piece, outer, n_out).reshape(-1, lanes)[: flat.shape[0]]
    part = gather_all(flat.reshape(part.shape), ring, n_ring).reshape((n_ring * each,) + part.shape[1:])
    return swap_halves_join(part, pair)


def pack_lower(m):
    h = m.shape[0] // 2
    top, low_right = m[:h, :h], m[h:, h:]
    folded = jnp.tril(top, -1) + low_right.T
    return jnp.concatenate([m[h:, :h], folded, jnp.diagonal(top)[None]], axis=0)


def unpack_lower(p):
    h = p.shape[-1]
    low_left, folded, diag = p[..., :h, :], p[..., h:2 * h, :], p[..., 2 * h, :]
    top = jnp.tril(folded, -1) + diag[..., :, None] * jnp.eye(h, dtype=p.dtype)
    low_right = jnp.swapaxes(jnp.triu(folded), -1, -2)
    upper = jnp.concatenate([top, jnp.zeros_like(top)], axis=-1)
    lower = jnp.concatenate([low_left, low_right], axis=-1)
    return jnp.concatenate([upper, lower], axis=-2)


def factor_inverse(gram):
    h = gram.shape[0] // 2
    eye = jnp.eye(h, dtype=gram.dtype)
    top = jnp.linalg.cholesky(gram[:h, :h])
    top_inv = lax.linalg.triangular_solve(top, eye, left_side=True, lower=True)
    low_left = jnp.dot(gram[h:, :h], top_inv.T, precision=HIGH)
    rest = gram[h:, h:] - jnp.dot(low_left, low_left.T, precision=HIGH)
    low = jnp.linalg.cholesky(rest)
    low_inv = lax.linalg.triangular_solve(low, eye, left_side=True, lower=True)
    mixed = -jnp.dot(low_inv, jnp.dot(low_left, top_inv, precision=HIGH), precision=HIGH)
    upper = jnp.concatenate([top_inv, jnp.zeros_like(top_inv)], axis=1)
    lower = jnp.concatenate([mixed, low_inv], axis=1)
    return jnp.concatenate([upper, lower], axis=0)


def on_device(hidden, sketch):
    states = hidden[0]
    projected = jnp.dot(states, sketch, preferred_element_type=jnp.float32).astype(jnp.bfloat16)
    basis_width = projected.shape[1]
    models = lax.axis_size("mdl")
    me = lax.axis_index("mdl")
    everyone = gather_all(projected, "mdl", models)
    local_tiles = jnp.einsum("ta,jtc->jac", projected, everyone, preferred_element_type=jnp.float32)
    tiles = sum_over_tokens(local_tiles, "c", "x", "z")
    gram_total = lax.dynamic_index_in_dim(tiles, me, 0, keepdims=False)
    inverse = factor_inverse(gram_total)
    packed = gather_all(pack_lower(inverse), "mdl", models)
    half = packed.shape[-1]
    low_left, folded, diag = packed[:, :half], packed[:, half:2 * half], packed[:, 2 * half]
    top = jnp.tril(folded, -1) + diag[:, :, None] * jnp.eye(half, dtype=packed.dtype)
    low_right_t = jnp.triu(folded)
    left_done = jnp.einsum("ab,jbc->jac", inverse, tiles, precision=lax.Precision.HIGH)
    first, second = left_done[..., :half], left_done[..., half:]
    out_first = jnp.einsum("jac,jdc->jad", first, top, precision=lax.Precision.HIGH)
    out_second = jnp.einsum("jac,jdc->jad", first, low_left, precision=lax.Precision.HIGH) + jnp.einsum(
        "jac,jcd->jad", second, low_right_t, precision=lax.Precision.HIGH)
    right_done = jnp.concatenate([out_first, out_second], axis=-1)
    cross_gram = right_done.transpose(1, 0, 2).reshape(basis_width, models * basis_width)
    similarity = jnp.sum(right_done * right_done, axis=(1, 2)) / basis_width
    return (cross_gram, similarity[None, :])


def solution(mesh):
    tok_size = mesh.shape["tok"]
    cores = 2
    z_size = tok_size // (4 * cores)
    devices = mesh.devices.reshape(tok_size // (z_size * cores), z_size, cores, mesh.shape["mdl"])
    sub = Mesh(devices, ("x", "z", "c", "mdl"))
    return jax.shard_map(
        on_device,
        mesh=sub,
        in_specs=(P("mdl", ("x", "z", "c"), None), P()),
        out_specs=(P("mdl", None), P("mdl", None)),
        check_vma=False,
    )
```

```python
import jax
import jax.numpy as jnp
from jax import lax
from jax.sharding import Mesh
from jax.sharding import PartitionSpec as P

HIGH = lax.Precision.HIGHEST


def scatter_sum(chunks, axes):
    return lax.all_to_all(chunks, axes, 0, 0, tiled=True).sum(axis=0)


def gather_all(piece, axes, count):
    copies = jnp.broadcast_to(piece[None], (count,) + piece.shape)
    return lax.all_to_all(copies, axes, 0, 0, tiled=True)


def swap_halves_sum(tiles, axis):
    side = lax.axis_index(axis)
    halves = tiles.reshape((2, tiles.shape[0] // 2) + tiles.shape[1:])
    mine = lax.dynamic_index_in_dim(halves, side, 0, keepdims=False)
    theirs = lax.dynamic_index_in_dim(halves, 1 - side, 0, keepdims=False)
    return mine + lax.ppermute(theirs, axis, [(0, 1), (1, 0)])


def sum_over_tokens(tiles, pair, ring, outer, lanes=128):
    n_ring = lax.axis_size(ring)
    n_out = lax.axis_size(outer)
    part = swap_halves_sum(tiles, pair)
    each = part.shape[0] // n_ring
    part = scatter_sum(part.reshape((n_ring, each) + part.shape[1:]), ring)
    flat = part.reshape(-1, lanes)
    pad = (-flat.shape[0]) % n_out
    padded = jnp.pad(flat, ((0, pad), (0, 0))).reshape(n_out, -1, lanes)
    piece = scatter_sum(padded, outer)
    flat = gather_all(piece, outer, n_out).reshape(-1, lanes)[: flat.shape[0]]
    return gather_all(flat.reshape(part.shape), ring, n_ring).reshape((n_ring * each,) + part.shape[1:])


def pack_lower(m):
    h = m.shape[0] // 2
    top, low_right = m[:h, :h], m[h:, h:]
    folded = jnp.tril(top, -1) + low_right.T
    return jnp.concatenate([m[h:, :h], folded, jnp.diagonal(top)[None]], axis=0)


def unpack_lower(p):
    h = p.shape[-1]
    low_left, folded, diag = p[..., :h, :], p[..., h:2 * h, :], p[..., 2 * h, :]
    top = jnp.tril(folded, -1) + diag[..., :, None] * jnp.eye(h, dtype=p.dtype)
    low_right = jnp.swapaxes(jnp.triu(folded), -1, -2)
    upper = jnp.concatenate([top, jnp.zeros_like(top)], axis=-1)
    lower = jnp.concatenate([low_left, low_right], axis=-1)
    return jnp.concatenate([upper, lower], axis=-2)


def factor_inverse(gram):
    h = gram.shape[0] // 2
    eye = jnp.eye(h, dtype=gram.dtype)
    top = jnp.linalg.cholesky(gram[:h, :h])
    top_inv = lax.linalg.triangular_solve(top, eye, left_side=True, lower=True)
    low_left = jnp.dot(gram[h:, :h], top_inv.T, precision=HIGH)
    rest = gram[h:, h:] - jnp.dot(low_left, low_left.T, precision=HIGH)
    low = jnp.linalg.cholesky(rest)
    low_inv = lax.linalg.triangular_solve(low, eye, left_side=True, lower=True)
    mixed = -jnp.dot(low_inv, jnp.dot(low_left, top_inv, precision=HIGH), precision=HIGH)
    upper = jnp.concatenate([top_inv, jnp.zeros_like(top_inv)], axis=1)
    lower = jnp.concatenate([mixed, low_inv], axis=1)
    return jnp.concatenate([upper, lower], axis=0)


def times_inverses_t(left_done, packed):
    half = packed.shape[-1]
    low_left, folded, diag = packed[:, :half], packed[:, half:2 * half], packed[:, 2 * half]
    top = jnp.tril(folded, -1) + diag[:, :, None] * jnp.eye(half, dtype=packed.dtype)
    low_right_t = jnp.triu(folded)
    first, second = left_done[..., :half], left_done[..., half:]
    out_first = jnp.einsum("jac,jdc->jad", first, top, precision=lax.Precision.HIGH)
    out_second = jnp.einsum("jac,jdc->jad", first, low_left, precision=lax.Precision.HIGH) + jnp.einsum(
        "jac,jcd->jad", second, low_right_t, precision=lax.Precision.HIGH)
    return jnp.concatenate([out_first, out_second], axis=-1)


def on_device(hidden, sketch):
    states = hidden[0]
    projected = jnp.dot(states, sketch, preferred_element_type=jnp.float32).astype(jnp.bfloat16)
    basis_width = projected.shape[1]
    models = lax.axis_size("mdl")
    me = lax.axis_index("mdl")
    side = lax.axis_index("c")
    everyone = gather_all(projected, "mdl", models)
    local_tiles = jnp.einsum("ta,jtc->jac", projected, everyone, preferred_element_type=jnp.float32)
    own = sum_over_tokens(local_tiles, "c", "x", "z")
    other = lax.ppermute(own, "c", [(0, 1), (1, 0)])
    each = own.shape[0]
    at = me % each
    mine_here = me // each == side
    gram_total = jnp.where(mine_here, lax.dynamic_index_in_dim(own, at, 0, keepdims=False),
                           lax.dynamic_index_in_dim(other, at, 0, keepdims=False))
    inverse = factor_inverse(gram_total)
    packed = gather_all(pack_lower(inverse), "mdl", models)
    packed_own = lax.dynamic_slice_in_dim(packed, side * each, each, 0)
    packed_other = lax.dynamic_slice_in_dim(packed, (1 - side) * each, each, 0)
    right_own = times_inverses_t(jnp.einsum("ab,jbc->jac", inverse, own, precision=lax.Precision.HIGH), packed_own)
    right_other = times_inverses_t(jnp.einsum("ab,jbc->jac", inverse, other, precision=lax.Precision.HIGH), packed_other)
    right_done = jnp.where(side == 0, jnp.concatenate([right_own, right_other], 0),
                           jnp.concatenate([right_other, right_own], 0))
    cross_gram = right_done.transpose(1, 0, 2).reshape(basis_width, models * basis_width)
    similarity = jnp.sum(right_done * right_done, axis=(1, 2)) / basis_width
    return (cross_gram, similarity[None, :])


def solution(mesh):
    tok_size = mesh.shape["tok"]
    cores = 2
    z_size = tok_size // (4 * cores)
    devices = mesh.devices.reshape(tok_size // (z_size * cores), z_size, cores, mesh.shape["mdl"])
    sub = Mesh(devices, ("x", "z", "c", "mdl"))
    return jax.shard_map(
        on_device,
        mesh=sub,
        in_specs=(P("mdl", ("x", "z", "c"), None), P()),
        out_specs=(P("mdl", None), P("mdl", None)),
        check_vma=False,
    )
```

```python
import jax
import jax.numpy as jnp
from jax import lax
from jax.sharding import Mesh
from jax.sharding import PartitionSpec as P

HIGH = lax.Precision.HIGHEST


def scatter_sum(chunks, axes):
    return lax.all_to_all(chunks, axes, 0, 0, tiled=True).sum(axis=0)


def gather_all(piece, axes, count):
    copies = jnp.broadcast_to(piece[None], (count,) + piece.shape)
    return lax.all_to_all(copies, axes, 0, 0, tiled=True)


def swap_halves_sum(tiles, axis):
    side = lax.axis_index(axis)
    halves = tiles.reshape((2, tiles.shape[0] // 2) + tiles.shape[1:])
    mine = lax.dynamic_index_in_dim(halves, side, 0, keepdims=False)
    theirs = lax.dynamic_index_in_dim(halves, 1 - side, 0, keepdims=False)
    return mine + lax.ppermute(theirs, axis, [(0, 1), (1, 0)])


def swap_halves_join(half, axis):
    side = lax.axis_index(axis)
    other = lax.ppermute(half, axis, [(0, 1), (1, 0)])
    return jnp.where(side == 0, jnp.concatenate([half, other], 0), jnp.concatenate([other, half], 0))


def sum_over_tokens(tiles, pair, ring, outer, lanes=128):
    n_ring = lax.axis_size(ring)
    n_out = lax.axis_size(outer)
    part = swap_halves_sum(tiles, pair)
    each = part.shape[0] // n_ring
    part = scatter_sum(part.reshape((n_ring, each) + part.shape[1:]), ring)
    flat = part.reshape(-1, lanes)
    pad = (-flat.shape[0]) % (n_out * 8)
    padded = jnp.pad(flat, ((0, pad), (0, 0))).reshape(n_out, -1, lanes)
    piece = scatter_sum(padded, outer)
    flat = gather_all(piece, outer, n_out).reshape(-1, lanes)[: flat.shape[0]]
    part = gather_all(flat.reshape(part.shape), ring, n_ring).reshape((n_ring * each,) + part.shape[1:])
    return swap_halves_join(part, pair)


def pack_lower(m):
    h = m.shape[0] // 2
    top, low_right = m[:h, :h], m[h:, h:]
    folded = jnp.tril(top, -1) + low_right.T
    return jnp.concatenate([m[h:, :h], folded, jnp.diagonal(top)[None]], axis=0)


def unpack_lower(p):
    h = p.shape[-1]
    low_left, folded, diag = p[..., :h, :], p[..., h:2 * h, :], p[..., 2 * h, :]
    top = jnp.tril(folded, -1) + diag[..., :, None] * jnp.eye(h, dtype=p.dtype)
    low_right = jnp.swapaxes(jnp.triu(folded), -1, -2)
    upper = jnp.concatenate([top, jnp.zeros_like(top)], axis=-1)
    lower = jnp.concatenate([low_left, low_right], axis=-1)
    return jnp.concatenate([upper, lower], axis=-2)


def factor_inverse(gram):
    h = gram.shape[0] // 2
    eye = jnp.eye(h, dtype=gram.dtype)
    top = jnp.linalg.cholesky(gram[:h, :h])
    top_inv = lax.linalg.triangular_solve(top, eye, left_side=True, lower=True)
    low_left = jnp.dot(gram[h:, :h], top_inv.T, precision=HIGH)
    rest = gram[h:, h:] - jnp.dot(low_left, low_left.T, precision=HIGH)
    low = jnp.linalg.cholesky(rest)
    low_inv = lax.linalg.triangular_solve(low, eye, left_side=True, lower=True)
    mixed = -jnp.dot(low_inv, jnp.dot(low_left, top_inv, precision=HIGH), precision=HIGH)
    upper = jnp.concatenate([top_inv, jnp.zeros_like(top_inv)], axis=1)
    lower = jnp.concatenate([mixed, low_inv], axis=1)
    return jnp.concatenate([upper, lower], axis=0)


def on_device(hidden, sketch):
    states = hidden[0]
    projected = jnp.dot(states, sketch, preferred_element_type=jnp.float32).astype(jnp.bfloat16)
    basis_width = projected.shape[1]
    models = lax.axis_size("mdl")
    me = lax.axis_index("mdl")
    everyone = gather_all(projected, "mdl", models)
    local_tiles = jnp.einsum("ta,jtc->jac", projected, everyone, preferred_element_type=jnp.float32)
    tiles = sum_over_tokens(local_tiles, "c", "x", "z")
    gram_total = lax.dynamic_index_in_dim(tiles, me, 0, keepdims=False)
    inverse = factor_inverse(gram_total)
    packed = gather_all(pack_lower(inverse), "mdl", models)
    half = packed.shape[-1]
    low_left, folded, diag = packed[:, :half], packed[:, half:2 * half], packed[:, 2 * half]
    top = jnp.tril(folded, -1) + diag[:, :, None] * jnp.eye(half, dtype=packed.dtype)
    low_right_t = jnp.triu(folded)
    left_done = jnp.einsum("ab,jbc->jac", inverse, tiles, precision=lax.Precision.HIGH)
    first, second = left_done[..., :half], left_done[..., half:]
    out_first = jnp.einsum("jac,jdc->jad", first, top, precision=lax.Precision.HIGH)
    out_second = jnp.einsum("jac,jdc->jad", first, low_left, precision=lax.Precision.HIGH) + jnp.einsum(
        "jac,jcd->jad", second, low_right_t, precision=lax.Precision.HIGH)
    right_done = jnp.concatenate([out_first, out_second], axis=-1)
    cross_gram = right_done.transpose(1, 0, 2).reshape(basis_width, models * basis_width)
    similarity = jnp.sum(right_done * right_done, axis=(1, 2)) / basis_width
    return (cross_gram, similarity[None, :])


def solution(mesh):
    tok_size = mesh.shape["tok"]
    cores = 2
    z_size = tok_size // (4 * cores)
    devices = mesh.devices.reshape(tok_size // (z_size * cores), z_size, cores, mesh.shape["mdl"])
    sub = Mesh(devices, ("x", "z", "c", "mdl"))
    return jax.shard_map(
        on_device,
        mesh=sub,
        in_specs=(P("mdl", ("x", "z", "c"), None), P()),
        out_specs=(P("mdl", None), P("mdl", None)),
        check_vma=False,
    )
```

```python
import jax
import jax.numpy as jnp
from jax import lax
from jax.sharding import Mesh
from jax.sharding import PartitionSpec as P

HIGH = lax.Precision.HIGHEST


def scatter_sum(chunks, axes):
    return lax.all_to_all(chunks, axes, 0, 0, tiled=True).sum(axis=0)


def gather_all(piece, axes, count):
    copies = jnp.broadcast_to(piece[None], (count,) + piece.shape)
    return lax.all_to_all(copies, axes, 0, 0, tiled=True)


def sum_over_tokens(tiles, pair, ring, outer, lanes=128):
    n_ring = lax.axis_size(ring)
    n_out = lax.axis_size(outer)
    part = scatter_sum(tiles.reshape((2, tiles.shape[0] // 2) + tiles.shape[1:]), pair)
    each = part.shape[0] // n_ring
    part = scatter_sum(part.reshape((n_ring, each) + part.shape[1:]), ring)
    flat = part.reshape(-1, lanes)
    pad = (-flat.shape[0]) % n_out
    padded = jnp.pad(flat, ((0, pad), (0, 0))).reshape(n_out, -1, lanes)
    piece = scatter_sum(padded, outer)
    flat = gather_all(piece, outer, n_out).reshape(-1, lanes)[: flat.shape[0]]
    part = gather_all(flat.reshape(part.shape), ring, n_ring).reshape((n_ring * each,) + part.shape[1:])
    return gather_all(part, pair, 2).reshape((2 * part.shape[0],) + part.shape[1:])


def pack_lower(m):
    h = m.shape[0] // 2
    top, low_right = m[:h, :h], m[h:, h:]
    folded = jnp.tril(top, -1) + low_right.T
    return jnp.concatenate([m[h:, :h], folded, jnp.diagonal(top)[None]], axis=0)


def unpack_lower(p):
    h = p.shape[-1]
    low_left, folded, diag = p[..., :h, :], p[..., h:2 * h, :], p[..., 2 * h, :]
    top = jnp.tril(folded, -1) + diag[..., :, None] * jnp.eye(h, dtype=p.dtype)
    low_right = jnp.swapaxes(jnp.triu(folded), -1, -2)
    upper = jnp.concatenate([top, jnp.zeros_like(top)], axis=-1)
    lower = jnp.concatenate([low_left, low_right], axis=-1)
    return jnp.concatenate([upper, lower], axis=-2)


def factor_inverse(gram):
    h = gram.shape[0] // 2
    eye = jnp.eye(h, dtype=gram.dtype)
    top = jnp.linalg.cholesky(gram[:h, :h])
    top_inv = lax.linalg.triangular_solve(top, eye, left_side=True, lower=True)
    low_left = jnp.dot(gram[h:, :h], top_inv.T, precision=HIGH)
    rest = gram[h:, h:] - jnp.dot(low_left, low_left.T, precision=HIGH)
    low = jnp.linalg.cholesky(rest)
    low_inv = lax.linalg.triangular_solve(low, eye, left_side=True, lower=True)
    mixed = -jnp.dot(low_inv, jnp.dot(low_left, top_inv, precision=HIGH), precision=HIGH)
    upper = jnp.concatenate([top_inv, jnp.zeros_like(top_inv)], axis=1)
    lower = jnp.concatenate([mixed, low_inv], axis=1)
    return jnp.concatenate([upper, lower], axis=0)


def on_device(hidden, sketch):
    states = hidden[0]
    projected = jnp.dot(states, sketch, preferred_element_type=jnp.float32).astype(jnp.bfloat16)
    basis_width = projected.shape[1]
    models = lax.axis_size("mdl")
    me = lax.axis_index("mdl")
    everyone = gather_all(projected, "mdl", models)
    local_tiles = jnp.einsum("ta,jtc->jac", projected, everyone, preferred_element_type=jnp.float32)
    tiles = sum_over_tokens(local_tiles, "c", "x", "z")
    gram_total = lax.dynamic_index_in_dim(tiles, me, 0, keepdims=False)
    inverse = factor_inverse(gram_total)
    packed = gather_all(pack_lower(inverse), "mdl", models)
    half = packed.shape[-1]
    low_left, folded, diag = packed[:, :half], packed[:, half:2 * half], packed[:, 2 * half]
    top = jnp.tril(folded, -1) + diag[:, :, None] * jnp.eye(half, dtype=packed.dtype)
    low_right_t = jnp.triu(folded)
    left_done = jnp.einsum("ab,jbc->jac", inverse, tiles, precision=lax.Precision.HIGH)
    first, second = left_done[..., :half], left_done[..., half:]
    out_first = jnp.einsum("jac,jdc->jad", first, top, precision=lax.Precision.HIGH)
    out_second = jnp.einsum("jac,jdc->jad", first, low_left, precision=lax.Precision.HIGH) + jnp.einsum(
        "jac,jcd->jad", second, low_right_t, precision=lax.Precision.HIGH)
    right_done = jnp.concatenate([out_first, out_second], axis=-1)
    cross_gram = right_done.transpose(1, 0, 2).reshape(basis_width, models * basis_width)
    similarity = jnp.sum(right_done * right_done, axis=(1, 2)) / basis_width
    return (cross_gram, similarity[None, :])


def solution(mesh):
    tok_size = mesh.shape["tok"]
    cores = 2
    z_size = tok_size // (4 * cores)
    devices = mesh.devices.reshape(tok_size // (z_size * cores), z_size, cores, mesh.shape["mdl"])
    sub = Mesh(devices, ("x", "z", "c", "mdl"))
    return jax.shard_map(
        on_device,
        mesh=sub,
        in_specs=(P("mdl", ("x", "z", "c"), None), P()),
        out_specs=(P("mdl", None), P("mdl", None)),
        check_vma=False,
    )
```

```python
import jax
import jax.numpy as jnp
from jax import lax
from jax.sharding import Mesh
from jax.sharding import PartitionSpec as P

HIGH = lax.Precision.HIGHEST


def scatter_sum(chunks, axes):
    return lax.all_to_all(chunks, axes, 0, 0, tiled=True).sum(axis=0)


def gather_all(piece, axes, count):
    copies = jnp.broadcast_to(piece[None], (count,) + piece.shape)
    return lax.all_to_all(copies, axes, 0, 0, tiled=True)


def swap_halves_sum(tiles, axis):
    side = lax.axis_index(axis)
    halves = tiles.reshape((2, tiles.shape[0] // 2) + tiles.shape[1:])
    mine = lax.dynamic_index_in_dim(halves, side, 0, keepdims=False)
    theirs = lax.dynamic_index_in_dim(halves, 1 - side, 0, keepdims=False)
    return mine + lax.ppermute(theirs, axis, [(0, 1), (1, 0)])


def swap_halves_join(half, axis):
    side = lax.axis_index(axis)
    other = lax.ppermute(half, axis, [(0, 1), (1, 0)])
    both = jnp.stack([half, other])
    order = jnp.stack([side, 1 - side])
    return jnp.take(both, order, axis=0).reshape((2 * half.shape[0],) + half.shape[1:])


def sum_over_tokens(tiles, pair, ring, outer, lanes=128):
    n_ring = lax.axis_size(ring)
    n_out = lax.axis_size(outer)
    part = swap_halves_sum(tiles, pair)
    each = part.shape[0] // n_ring
    part = scatter_sum(part.reshape((n_ring, each) + part.shape[1:]), ring)
    flat = part.reshape(-1, lanes)
    pad = (-flat.shape[0]) % n_out
    padded = jnp.pad(flat, ((0, pad), (0, 0))).reshape(n_out, -1, lanes)
    piece = scatter_sum(padded, outer)
    flat = gather_all(piece, outer, n_out).reshape(-1, lanes)[: flat.shape[0]]
    part = gather_all(flat.reshape(part.shape), ring, n_ring).reshape((n_ring * each,) + part.shape[1:])
    return swap_halves_join(part, pair)


def pack_lower(m):
    h = m.shape[0] // 2
    top, low_right = m[:h, :h], m[h:, h:]
    folded = jnp.tril(top, -1) + low_right.T
    return jnp.concatenate([m[h:, :h], folded, jnp.diagonal(top)[None]], axis=0)


def unpack_lower(p):
    h = p.shape[-1]
    low_left, folded, diag = p[..., :h, :], p[..., h:2 * h, :], p[..., 2 * h, :]
    top = jnp.tril(folded, -1) + diag[..., :, None] * jnp.eye(h, dtype=p.dtype)
    low_right = jnp.swapaxes(jnp.triu(folded), -1, -2)
    upper = jnp.concatenate([top, jnp.zeros_like(top)], axis=-1)
    lower = jnp.concatenate([low_left, low_right], axis=-1)
    return jnp.concatenate([upper, lower], axis=-2)


def factor_inverse(gram):
    h = gram.shape[0] // 2
    eye = jnp.eye(h, dtype=gram.dtype)
    top = jnp.linalg.cholesky(gram[:h, :h])
    top_inv = lax.linalg.triangular_solve(top, eye, left_side=True, lower=True)
    low_left = jnp.dot(gram[h:, :h], top_inv.T, precision=HIGH)
    rest = gram[h:, h:] - jnp.dot(low_left, low_left.T, precision=HIGH)
    low = jnp.linalg.cholesky(rest)
    low_inv = lax.linalg.triangular_solve(low, eye, left_side=True, lower=True)
    mixed = -jnp.dot(low_inv, jnp.dot(low_left, top_inv, precision=HIGH), precision=HIGH)
    upper = jnp.concatenate([top_inv, jnp.zeros_like(top_inv)], axis=1)
    lower = jnp.concatenate([mixed, low_inv], axis=1)
    return jnp.concatenate([upper, lower], axis=0)


def on_device(hidden, sketch):
    states = hidden[0]
    projected = jnp.dot(states, sketch, preferred_element_type=jnp.float32).astype(jnp.bfloat16)
    basis_width = projected.shape[1]
    models = lax.axis_size("mdl")
    me = lax.axis_index("mdl")
    everyone = gather_all(projected, "mdl", models)
    local_tiles = jnp.einsum("ta,jtc->jac", projected, everyone, preferred_element_type=jnp.float32)
    tiles = sum_over_tokens(local_tiles, "c", "x", "z")
    gram_total = lax.dynamic_index_in_dim(tiles, me, 0, keepdims=False)
    inverse = factor_inverse(gram_total)
    packed = gather_all(pack_lower(inverse), "mdl", models)
    half = packed.shape[-1]
    low_left, folded, diag = packed[:, :half], packed[:, half:2 * half], packed[:, 2 * half]
    top = jnp.tril(folded, -1) + diag[:, :, None] * jnp.eye(half, dtype=packed.dtype)
    low_right_t = jnp.triu(folded)
    left_done = jnp.einsum("ab,jbc->jac", inverse, tiles, precision=lax.Precision.HIGH)
    first, second = left_done[..., :half], left_done[..., half:]
    out_first = jnp.einsum("jac,jdc->jad", first, top, precision=lax.Precision.HIGH)
    out_second = jnp.einsum("jac,jdc->jad", first, low_left, precision=lax.Precision.HIGH) + jnp.einsum(
        "jac,jcd->jad", second, low_right_t, precision=lax.Precision.HIGH)
    right_done = jnp.concatenate([out_first, out_second], axis=-1)
    cross_gram = right_done.transpose(1, 0, 2).reshape(basis_width, models * basis_width)
    similarity = jnp.sum(right_done * right_done, axis=(1, 2)) / basis_width
    return (cross_gram, similarity[None, :])


def solution(mesh):
    tok_size = mesh.shape["tok"]
    cores = 2
    z_size = tok_size // (4 * cores)
    devices = mesh.devices.reshape(tok_size // (z_size * cores), z_size, cores, mesh.shape["mdl"])
    sub = Mesh(devices, ("x", "z", "c", "mdl"))
    return jax.shard_map(
        on_device,
        mesh=sub,
        in_specs=(P("mdl", ("x", "z", "c"), None), P()),
        out_specs=(P("mdl", None), P("mdl", None)),
        check_vma=False,
    )
```

```python
import jax
import jax.numpy as jnp
from jax import lax
from jax.sharding import Mesh
from jax.sharding import PartitionSpec as P

HIGH = lax.Precision.HIGH


def scatter_sum(chunks, axes):
    return lax.all_to_all(chunks, axes, 0, 0, tiled=True).sum(axis=0)


def gather_all(piece, axes, count):
    copies = jnp.broadcast_to(piece[None], (count,) + piece.shape)
    return lax.all_to_all(copies, axes, 0, 0, tiled=True)


def swap_halves_sum(tiles, axis):
    side = lax.axis_index(axis)
    halves = tiles.reshape((2, tiles.shape[0] // 2) + tiles.shape[1:])
    mine = lax.dynamic_index_in_dim(halves, side, 0, keepdims=False)
    theirs = lax.dynamic_index_in_dim(halves, 1 - side, 0, keepdims=False)
    return mine + lax.ppermute(theirs, axis, [(0, 1), (1, 0)])


def swap_halves_join(half, axis):
    side = lax.axis_index(axis)
    other = lax.ppermute(half, axis, [(0, 1), (1, 0)])
    return jnp.where(side == 0, jnp.concatenate([half, other], 0), jnp.concatenate([other, half], 0))


def sum_over_tokens(tiles, pair, ring, outer, lanes=128):
    n_ring = lax.axis_size(ring)
    n_out = lax.axis_size(outer)
    part = swap_halves_sum(tiles, pair)
    each = part.shape[0] // n_ring
    part = scatter_sum(part.reshape((n_ring, each) + part.shape[1:]), ring)
    flat = part.reshape(-1, lanes)
    pad = (-flat.shape[0]) % n_out
    padded = jnp.pad(flat, ((0, pad), (0, 0))).reshape(n_out, -1, lanes)
    piece = scatter_sum(padded, outer)
    flat = gather_all(piece, outer, n_out).reshape(-1, lanes)[: flat.shape[0]]
    part = gather_all(flat.reshape(part.shape), ring, n_ring).reshape((n_ring * each,) + part.shape[1:])
    return swap_halves_join(part, pair)


def pack_lower(m):
    h = m.shape[0] // 2
    top, low_right = m[:h, :h], m[h:, h:]
    folded = jnp.tril(top, -1) + low_right.T
    return jnp.concatenate([m[h:, :h], folded, jnp.diagonal(top)[None]], axis=0)


def unpack_lower(p):
    h = p.shape[-1]
    low_left, folded, diag = p[..., :h, :], p[..., h:2 * h, :], p[..., 2 * h, :]
    top = jnp.tril(folded, -1) + diag[..., :, None] * jnp.eye(h, dtype=p.dtype)
    low_right = jnp.swapaxes(jnp.triu(folded), -1, -2)
    upper = jnp.concatenate([top, jnp.zeros_like(top)], axis=-1)
    lower = jnp.concatenate([low_left, low_right], axis=-1)
    return jnp.concatenate([upper, lower], axis=-2)


def factor_inverse(gram):
    h = gram.shape[0] // 2
    eye = jnp.eye(h, dtype=gram.dtype)
    top = jnp.linalg.cholesky(gram[:h, :h])
    top_inv = lax.linalg.triangular_solve(top, eye, left_side=True, lower=True)
    low_left = jnp.dot(gram[h:, :h], top_inv.T, precision=HIGH)
    rest = gram[h:, h:] - jnp.dot(low_left, low_left.T, precision=HIGH)
    low = jnp.linalg.cholesky(rest)
    low_inv = lax.linalg.triangular_solve(low, eye, left_side=True, lower=True)
    mixed = -jnp.dot(low_inv, jnp.dot(low_left, top_inv, precision=HIGH), precision=HIGH)
    upper = jnp.concatenate([top_inv, jnp.zeros_like(top_inv)], axis=1)
    lower = jnp.concatenate([mixed, low_inv], axis=1)
    return jnp.concatenate([upper, lower], axis=0)


def on_device(hidden, sketch):
    states = hidden[0]
    projected = jnp.dot(states, sketch, preferred_element_type=jnp.float32).astype(jnp.bfloat16)
    basis_width = projected.shape[1]
    models = lax.axis_size("mdl")
    me = lax.axis_index("mdl")
    everyone = gather_all(projected, "mdl", models)
    local_tiles = jnp.einsum("ta,jtc->jac", projected, everyone, preferred_element_type=jnp.float32)
    tiles = sum_over_tokens(local_tiles, "c", "x", "z")
    gram_total = lax.dynamic_index_in_dim(tiles, me, 0, keepdims=False)
    inverse = factor_inverse(gram_total)
    packed = gather_all(pack_lower(inverse), "mdl", models)
    half = packed.shape[-1]
    low_left, folded, diag = packed[:, :half], packed[:, half:2 * half], packed[:, 2 * half]
    top = jnp.tril(folded, -1) + diag[:, :, None] * jnp.eye(half, dtype=packed.dtype)
    low_right_t = jnp.triu(folded)
    left_done = jnp.einsum("ab,jbc->jac", inverse, tiles, precision=lax.Precision.HIGH)
    first, second = left_done[..., :half], left_done[..., half:]
    out_first = jnp.einsum("jac,jdc->jad", first, top, precision=lax.Precision.HIGH)
    out_second = jnp.einsum("jac,jdc->jad", first, low_left, precision=lax.Precision.HIGH) + jnp.einsum(
        "jac,jcd->jad", second, low_right_t, precision=lax.Precision.HIGH)
    right_done = jnp.concatenate([out_first, out_second], axis=-1)
    cross_gram = right_done.transpose(1, 0, 2).reshape(basis_width, models * basis_width)
    similarity = jnp.sum(right_done * right_done, axis=(1, 2)) / basis_width
    return (cross_gram, similarity[None, :])


def solution(mesh):
    tok_size = mesh.shape["tok"]
    cores = 2
    z_size = tok_size // (4 * cores)
    devices = mesh.devices.reshape(tok_size // (z_size * cores), z_size, cores, mesh.shape["mdl"])
    sub = Mesh(devices, ("x", "z", "c", "mdl"))
    return jax.shard_map(
        on_device,
        mesh=sub,
        in_specs=(P("mdl", ("x", "z", "c"), None), P()),
        out_specs=(P("mdl", None), P("mdl", None)),
        check_vma=False,
    )
```
